1024 devices in a mesh: dp: 16 (over y, x_hi), pipe: 8 (over x_lo, core), seq: 8 (over z).
Axes of the slice: x: 8 (x_hi: 2, x_lo: 4; x = x_hi * 4 + x_lo), y: 8, z: 8, core: 2. Of those that a mesh axis runs over, the one named last changes fastest.
Arguments:
- query_proj: bfloat16 [8, 16, 1024, 2048], P('pipe', 'dp', 'seq'), may hold values from -6 to 6
- key_proj: bfloat16 [8, 16, 1024, 1024], P('pipe', 'dp', 'seq'), may hold values from -6 to 6
- value_proj: bfloat16 [8, 16, 1024, 1024], P('pipe', 'dp', 'seq'), may hold values from -24 to 24
- out_grad: bfloat16 [8, 16, 1024, 2048], P('pipe', 'dp', 'seq'), may hold values from -12 to 12
- lowest_key_index: int32 [8, 16, 1024], P('pipe', 'dp'), may hold values from 0 to 1023, as said below
- query_gain: float32 [8, 128], P('pipe'), may hold values from 0.1 to 1.9
- key_gain: float32 [8, 128], P('pipe'), may hold values from 0.1 to 1.9
Outputs:
- query_grad: bfloat16 [8, 16, 1024, 2048], P('pipe', 'dp', 'seq')
- key_grad: bfloat16 [8, 16, 1024, 1024], P('pipe', 'dp', 'seq')
- value_grad: bfloat16 [8, 16, 1024, 1024], P('pipe', 'dp', 'seq')
- query_gain_grad: float32 [8, 128], P('pipe')
- key_gain_grad: float32 [8, 128], P('pipe')
The draws below stay inside these ranges and needn't reach their ends.
Inputs may be any that keep to these rules, and one draw needn't show every extreme that they name: Query i may see keys lowest_key_index[i] to i: lowest_key_index never decreases along the tokens of a block, lowest_key_index[i] <= i and i - lowest_key_index[i] < 128; lowest_key_index[i] is i - 127 or the first token of i's document, whichever is larger.
All inputs are finite; a program needn't handle non-finite values.
Results may differ from the reference program's by a relative error of at most 0.0073.
Values may be sent and summed in bfloat16 or wider, within the bound.
No kernel may reach another device: no remote copies, remote signals or barrier semaphores. Data moves between devices by JAX's collectives and lax.ppermute only.
A program may use at most 32 MiB of HBM per device.

```python
import jax
import jax.numpy as jnp
from jax import lax

HQ = 16
KVH = 8
HD = 128
WINDOW = 128
SECTIONS = 8
REPLICAS = 16
TOKENS = 1024


def draw_lowest_key_index(key, part):
    flags = jax.random.randint(key, (SECTIONS, REPLICAS, TOKENS), 0, TOKENS // 2)
    places = jnp.arange(TOKENS, dtype=jnp.int32)
    opening = (flags == 0) | (places == 0) | (places == TOKENS - 1)
    starts = jnp.where(opening, places, jnp.zeros_like(flags))
    doc_start = lax.cummax(starts, axis=2)
    return jnp.maximum(doc_start, places - (WINDOW - 1)).astype(jnp.int32)


def level_of(key, shape, shards, low, largest):
    loudness = 1.0
    for dim, blocks in shards:
        draws = jax.random.uniform(jax.random.fold_in(jax.random.fold_in(key, 6), dim), (blocks,), jnp.float32, low / len(shards), largest / len(shards))
        loudness = loudness * jnp.repeat(jnp.exp(draws), shape[dim] // blocks).reshape((-1,) + (1,) * (len(shape) - 1 - dim))
    return loudness


def scatter_about(key, extent, scale, bound, shards=(), held_as=jnp.bfloat16):
    level = level_of(key, extent, shards, -0.22, 0.18) if shards else 1.0
    result = jax.random.normal(key, extent, jnp.float32) * scale * level
    return jnp.minimum(jnp.maximum(result, -bound), bound).astype(held_as)


def setup_inputs(seed: int = 0) -> dict:
    seeds = jax.random.split(jax.random.key(seed), 8)
    query_proj = scatter_about(seeds[0], (SECTIONS, REPLICAS, TOKENS, HQ * HD), 1.0, 6.0, ((0, 8), (1, 16), (2, 8)))
    key_proj = scatter_about(seeds[1], (SECTIONS, REPLICAS, TOKENS, KVH * HD), 1.0, 6.0, ((0, 8), (1, 16), (2, 8)))
    value_proj = scatter_about(seeds[2], (SECTIONS, REPLICAS, TOKENS, KVH * HD), 4.0, 24.0, ((0, 8), (1, 16), (2, 8)))
    out_grad = scatter_about(seeds[3], (SECTIONS, REPLICAS, TOKENS, HQ * HD), 2.0, 12.0, ((0, 8), (1, 16), (2, 8)))
    lowest_key_index = draw_lowest_key_index(jax.random.fold_in(seeds[7], 71), 0)
    query_gain = jnp.clip(1.0 + 0.18 * jax.random.normal(seeds[5], (SECTIONS, HD), jnp.float32), 0.1, 1.9)
    key_gain = jnp.clip(1.0 + 0.18 * jax.random.normal(seeds[6], (SECTIONS, HD), jnp.float32), 0.1, 1.9)
    return {"query_proj": query_proj, "key_proj": key_proj, "value_proj": value_proj, "out_grad": out_grad, "lowest_key_index": lowest_key_index, "query_gain": query_gain, "key_gain": key_gain}


epsilon = 1e-06
score_scale = 168.0 ** (-0.5)

def normalize(values, gain):
    inverse = lax.rsqrt(lax.optimization_barrier(jnp.mean(values * values, axis=-1, keepdims=True)) + epsilon)
    unit = values * inverse
    normed = lax.optimization_barrier((unit * gain).astype(jnp.bfloat16))
    return (unit, inverse, normed)

def norm_back(grad_normed, unit, inverse, gain):
    grad_unit = grad_normed * gain
    centered = grad_unit - unit * lax.optimization_barrier(jnp.mean(grad_unit * unit, axis=-1, keepdims=True))
    return inverse * centered

def group_attention(operands, lowest_key_index):
    queries, keys_in, values_in, upstream = operands
    places = jnp.arange(TOKENS, dtype=jnp.int32)
    visible = (places[None, :] <= places[:, None]) & (places[None, :] >= lowest_key_index[:, None])
    query_f = queries.astype(jnp.float32)
    key_f = keys_in.astype(jnp.float32)
    value_f = values_in.astype(jnp.float32)
    upstream_f = upstream.astype(jnp.float32)
    scores = jnp.einsum('rtd,sd->rts', query_f, key_f) * score_scale
    exp_scores = jnp.where(visible[None], jnp.exp(scores), jnp.zeros_like(scores))
    weights = exp_scores / lax.optimization_barrier(jnp.sum(exp_scores, axis=-1, keepdims=True))
    weights_reduced = lax.optimization_barrier(weights.astype(jnp.bfloat16)).astype(jnp.float32)
    attended = jnp.einsum('rts,sd->rtd', weights_reduced, value_f)
    delta_row = lax.optimization_barrier(jnp.sum(upstream_f * attended, axis=-1, keepdims=True))
    prob_grad = jnp.einsum('rtd,sd->rts', upstream_f, value_f)
    logit_gradient = weights * (prob_grad - delta_row) * score_scale
    logit_gradient = lax.optimization_barrier(logit_gradient.astype(jnp.bfloat16)).astype(jnp.float32)
    query_normed_grad = jnp.einsum('rts,sd->rtd', logit_gradient, key_f)
    key_normed_grad = jnp.einsum('rts,rtd->sd', logit_gradient, query_f)
    value_grad = jnp.einsum('rts,rtd->sd', weights_reduced, upstream_f)
    return (query_normed_grad, key_normed_grad, value_grad)

def one_item(operands):
    query_proj, key_proj, value_proj, upstream, lowest_key_index, query_gain, key_gain = operands
    ratio = HQ // KVH
    query_unit, query_inverse, query_normed = normalize(query_proj.astype(jnp.float32).reshape(TOKENS, HQ, HD), query_gain)
    key_unit, key_inverse, key_normed = normalize(key_proj.astype(jnp.float32).reshape(TOKENS, KVH, HD), key_gain)
    grouped_query = query_normed.reshape(TOKENS, KVH, ratio, HD).transpose(1, 2, 0, 3)
    grouped_key = key_normed.transpose(1, 0, 2)
    grouped_value = value_proj.reshape(TOKENS, KVH, HD).transpose(1, 0, 2)
    grouped_up = upstream.reshape(TOKENS, KVH, ratio, HD).transpose(1, 2, 0, 3)

    def inner(group_ops):
        return group_attention(group_ops, lowest_key_index)
    query_parts, key_parts, value_parts = lax.map(inner, (grouped_query, grouped_key, grouped_value, grouped_up))
    query_normed_grad = query_parts.transpose(2, 0, 1, 3).reshape(TOKENS, HQ, HD)
    key_normed_grad = key_parts.transpose(1, 0, 2)
    query_grad = norm_back(query_normed_grad, query_unit, query_inverse, query_gain).astype(jnp.bfloat16).reshape(TOKENS, HQ * HD)
    key_grad = norm_back(key_normed_grad, key_unit, key_inverse, key_gain).astype(jnp.bfloat16).reshape(TOKENS, KVH * HD)
    value_grad = value_parts.transpose(1, 0, 2).reshape(TOKENS, KVH * HD).astype(jnp.bfloat16)
    query_term = lax.optimization_barrier(jnp.sum(query_normed_grad * query_unit, axis=(0, 1)))
    key_term = lax.optimization_barrier(jnp.sum(key_normed_grad * key_unit, axis=(0, 1)))
    return (query_grad, key_grad, value_grad, query_term, key_term)

def reference(query_proj, key_proj, value_proj, out_grad, lowest_key_index, query_gain, key_gain):
    upstream = jnp.roll(out_grad, -1, axis=0)
    items = SECTIONS * REPLICAS
    operands = (query_proj.reshape(items, TOKENS, HQ * HD), key_proj.reshape(items, TOKENS, KVH * HD), value_proj.reshape(items, TOKENS, KVH * HD), upstream.reshape(items, TOKENS, HQ * HD), lowest_key_index.reshape(items, TOKENS), jnp.repeat(query_gain, REPLICAS, axis=0), jnp.repeat(key_gain, REPLICAS, axis=0))
    query_grad, key_grad, value_grad, query_term, key_term = lax.map(one_item, operands)
    return (query_grad.reshape(SECTIONS, REPLICAS, TOKENS, HQ * HD), key_grad.reshape(SECTIONS, REPLICAS, TOKENS, KVH * HD), value_grad.reshape(SECTIONS, REPLICAS, TOKENS, KVH * HD), lax.optimization_barrier(jnp.sum(query_term.reshape(SECTIONS, REPLICAS, HD), axis=1)), lax.optimization_barrier(jnp.sum(key_term.reshape(SECTIONS, REPLICAS, HD), axis=1)))
```

```python
import jax
import jax.numpy as jnp
from jax import lax
from jax.sharding import PartitionSpec as P

WINDOW = 128


epsilon = 1e-06
score_scale = 168.0 ** (-0.5)


def passed_along(x, axis, by):
    devices = lax.axis_size(axis)
    return lax.ppermute(x, axis, [(i, (i + by) % devices) for i in range(devices)])


def normalize(values, gain):
    inverse = lax.rsqrt(jnp.mean(values * values, axis=-1, keepdims=True) + epsilon)
    unit = values * inverse
    return (unit, inverse, (unit * gain).astype(jnp.bfloat16))


def norm_back(grad_normed, unit, inverse, gain):
    grad_unit = grad_normed * gain
    centered = grad_unit - unit * jnp.mean(grad_unit * unit, axis=-1, keepdims=True)
    return inverse * centered


def on_device(query_proj, key_proj, value_proj, out_grad, lowest_key_index, query_gain, key_gain):
    local_tokens = query_proj.shape[2]
    query_width = query_proj.shape[3]
    key_width = key_proj.shape[3]
    query_local = query_proj.reshape(local_tokens, query_width)
    key_local = key_proj.reshape(local_tokens, key_width)
    value_local = value_proj.reshape(local_tokens, key_width)
    grad_local = out_grad.reshape(local_tokens, query_width)
    arrived = passed_along(grad_local, "pipe", -1)
    query_heads, key_heads, value_heads = (
        lax.all_to_all(query_local, "seq", split_axis=1, concat_axis=0, tiled=True),
        lax.all_to_all(key_local, "seq", split_axis=1, concat_axis=0, tiled=True),
        lax.all_to_all(value_local, "seq", split_axis=1, concat_axis=0, tiled=True),
    )
    grad_heads = lax.all_to_all(arrived, "seq", split_axis=1, concat_axis=0, tiled=True)
    total = query_heads.shape[0]
    head_dim = query_gain.shape[1]
    groups = key_heads.shape[1] // head_dim
    ratio = query_heads.shape[1] // (groups * head_dim)
    floor_row = lowest_key_index.reshape(total)
    query_scale = query_gain.reshape(head_dim)
    key_scale = key_gain.reshape(head_dim)
    query_unit, query_inverse, query_normed = normalize(
        query_heads.astype(jnp.float32).reshape(total, groups, ratio, head_dim), query_scale
    )
    key_unit, key_inverse, key_normed = normalize(
        key_heads.astype(jnp.float32).reshape(total, groups, head_dim), key_scale
    )
    query_lay = jnp.transpose(query_normed, (1, 2, 0, 3))
    grad_lay = jnp.transpose(grad_heads.reshape(total, groups, ratio, head_dim), (1, 2, 0, 3))
    key_lay = jnp.transpose(key_normed, (1, 0, 2))
    value_lay = jnp.transpose(value_heads.reshape(total, groups, head_dim), (1, 0, 2))
    block_rows = 2 * WINDOW
    query_parts = []
    key_acc = jnp.zeros((groups, total, head_dim), jnp.float32)
    value_acc = jnp.zeros((groups, total, head_dim), jnp.float32)
    for block in range(total // block_rows):
        first = block * block_rows
        stop = first + block_rows
        key_first = max(first - WINDOW, 0)
        query_tile = query_lay[:, :, first:stop]
        grad_tile = grad_lay[:, :, first:stop]
        key_tile = key_lay[:, key_first:stop]
        value_tile = value_lay[:, key_first:stop]
        key_places = jnp.arange(key_first, stop, dtype=jnp.int32)
        query_places = jnp.arange(first, stop, dtype=jnp.int32)
        visible = (key_places[None, :] <= query_places[:, None]) & (
            key_places[None, :] >= floor_row[first:stop, None]
        )
        scores = (
            jnp.einsum("grqd,gkd->grqk", query_tile, key_tile, preferred_element_type=jnp.float32)
            * score_scale
        )
        exp_scores = jnp.where(visible, jnp.exp(scores), jnp.zeros_like(scores))
        weights = exp_scores / jnp.sum(exp_scores, axis=-1, keepdims=True)
        weights_reduced = weights.astype(jnp.bfloat16)
        attended = jnp.einsum(
            "grqk,gkd->grqd", weights_reduced, value_tile, preferred_element_type=jnp.float32
        )
        delta_col = jnp.sum(grad_tile.astype(jnp.float32) * attended, axis=-1, keepdims=True)
        prob_grad = jnp.einsum(
            "grqd,gkd->grqk", grad_tile, value_tile, preferred_element_type=jnp.float32
        )
        logit_gradient = (weights * (prob_grad - delta_col) * score_scale).astype(jnp.bfloat16)
        query_parts.append(
            jnp.einsum(
                "grqk,gkd->grqd", logit_gradient, key_tile, preferred_element_type=jnp.float32
            )
        )
        key_acc = key_acc.at[:, key_first:stop].add(
            jnp.einsum(
                "grqk,grqd->gkd", logit_gradient, query_tile, preferred_element_type=jnp.float32
            )
        )
        value_acc = value_acc.at[:, key_first:stop].add(
            jnp.einsum(
                "grqk,grqd->gkd", weights_reduced, grad_tile, preferred_element_type=jnp.float32
            )
        )
    query_normed_grad = jnp.transpose(jnp.concatenate(query_parts, axis=2), (2, 0, 1, 3))
    key_normed_grad = jnp.transpose(key_acc, (1, 0, 2))
    value_rows = jnp.transpose(value_acc, (1, 0, 2))
    query_grad = (
        norm_back(query_normed_grad, query_unit, query_inverse, query_scale)
        .astype(jnp.bfloat16)
        .reshape(total, groups * ratio * head_dim)
    )
    key_grad = (
        norm_back(key_normed_grad, key_unit, key_inverse, key_scale)
        .astype(jnp.bfloat16)
        .reshape(total, groups * head_dim)
    )
    value_grad = value_rows.astype(jnp.bfloat16).reshape(total, groups * head_dim)
    query_term = jnp.sum(query_normed_grad * query_unit, axis=(0, 1, 2))
    key_term = jnp.sum(key_normed_grad * key_unit, axis=(0, 1))
    pipe_index = lax.axis_index("pipe")
    slots = jnp.zeros((lax.axis_size("pipe"), 2, head_dim), jnp.float32)
    slots = lax.dynamic_update_slice(slots, jnp.stack([query_term, key_term])[None], (pipe_index, 0, 0))
    summed = lax.psum(slots, ("dp", "pipe", "seq"))
    picked = lax.dynamic_slice(summed, (pipe_index, 0, 0), (1, 2, head_dim))
    query_sum, key_sum = picked[0, 0], picked[0, 1]
    query_back, key_back, value_back = (
        lax.all_to_all(query_grad, "seq", split_axis=0, concat_axis=1, tiled=True),
        lax.all_to_all(key_grad, "seq", split_axis=0, concat_axis=1, tiled=True),
        lax.all_to_all(value_grad, "seq", split_axis=0, concat_axis=1, tiled=True),
    )
    return (
        query_back.reshape(1, 1, local_tokens, query_width),
        key_back.reshape(1, 1, local_tokens, key_width),
        value_back.reshape(1, 1, local_tokens, key_width),
        query_sum.reshape(1, head_dim),
        key_sum.reshape(1, head_dim),
    )


def solution(mesh):
    return jax.shard_map(
        on_device,
        mesh=mesh,
        in_specs=(
            P("pipe", "dp", "seq", None),
            P("pipe", "dp", "seq", None),
            P("pipe", "dp", "seq", None),
            P("pipe", "dp", "seq", None),
            P("pipe", "dp", None),
            P("pipe", None),
            P("pipe", None),
        ),
        out_specs=(
            P("pipe", "dp", "seq", None),
            P("pipe", "dp", "seq", None),
            P("pipe", "dp", "seq", None),
            P("pipe", None),
            P("pipe", None),
        ),
        check_vma=False,
    )
```

```python
import jax
import jax.numpy as jnp
from jax import lax
from jax.sharding import PartitionSpec as P

WINDOW = 128


epsilon = 1e-06
score_scale = 168.0 ** (-0.5)


def passed_along(x, axis, by):
    devices = lax.axis_size(axis)
    return lax.ppermute(x, axis, [(i, (i + by) % devices) for i in range(devices)])


def summed_over(x, axes):
    for axis in axes:
        devices = lax.axis_size(axis)
        step = 1
        while step < devices:
            x = x + lax.ppermute(x, axis, [(i, i ^ step) for i in range(devices)])
            step *= 2
    return x


def normalize(values, gain):
    inverse = lax.rsqrt(jnp.mean(values * values, axis=-1, keepdims=True) + epsilon)
    unit = values * inverse
    return (unit, inverse, (unit * gain).astype(jnp.bfloat16))


def norm_back(grad_normed, unit, inverse, gain):
    grad_unit = grad_normed * gain
    centered = grad_unit - unit * jnp.mean(grad_unit * unit, axis=-1, keepdims=True)
    return inverse * centered


def on_device(query_proj, key_proj, value_proj, out_grad, lowest_key_index, query_gain, key_gain):
    local_tokens = query_proj.shape[2]
    query_width = query_proj.shape[3]
    key_width = key_proj.shape[3]
    query_local = query_proj.reshape(local_tokens, query_width)
    key_local = key_proj.reshape(local_tokens, key_width)
    value_local = value_proj.reshape(local_tokens, key_width)
    grad_local = out_grad.reshape(local_tokens, query_width)
    arrived = passed_along(grad_local, "pipe", -1)
    query_heads, key_heads, value_heads = (
        lax.all_to_all(query_local, "seq", split_axis=1, concat_axis=0, tiled=True),
        lax.all_to_all(key_local, "seq", split_axis=1, concat_axis=0, tiled=True),
        lax.all_to_all(value_local, "seq", split_axis=1, concat_axis=0, tiled=True),
    )
    grad_heads = lax.all_to_all(arrived, "seq", split_axis=1, concat_axis=0, tiled=True)
    total = query_heads.shape[0]
    head_dim = query_gain.shape[1]
    groups = key_heads.shape[1] // head_dim
    ratio = query_heads.shape[1] // (groups * head_dim)
    floor_row = lowest_key_index.reshape(total)
    query_scale = query_gain.reshape(head_dim)
    key_scale = key_gain.reshape(head_dim)
    query_unit, query_inverse, query_normed = normalize(
        query_heads.astype(jnp.float32).reshape(total, groups, ratio, head_dim), query_scale
    )
    key_unit, key_inverse, key_normed = normalize(
        key_heads.astype(jnp.float32).reshape(total, groups, head_dim), key_scale
    )
    query_lay = jnp.transpose(query_normed, (1, 2, 0, 3))
    grad_lay = jnp.transpose(grad_heads.reshape(total, groups, ratio, head_dim), (1, 2, 0, 3))
    key_lay = jnp.transpose(key_normed, (1, 0, 2))
    value_lay = jnp.transpose(value_heads.reshape(total, groups, head_dim), (1, 0, 2))
    block_rows = 2 * WINDOW
    query_parts = []
    key_acc = jnp.zeros((groups, total, head_dim), jnp.float32)
    value_acc = jnp.zeros((groups, total, head_dim), jnp.float32)
    for block in range(total // block_rows):
        first = block * block_rows
        stop = first + block_rows
        key_first = max(first - WINDOW, 0)
        query_tile = query_lay[:, :, first:stop]
        grad_tile = grad_lay[:, :, first:stop]
        key_tile = key_lay[:, key_first:stop]
        value_tile = value_lay[:, key_first:stop]
        key_places = jnp.arange(key_first, stop, dtype=jnp.int32)
        query_places = jnp.arange(first, stop, dtype=jnp.int32)
        visible = (key_places[None, :] <= query_places[:, None]) & (
            key_places[None, :] >= floor_row[first:stop, None]
        )
        scores = (
            jnp.einsum("grqd,gkd->grqk", query_tile, key_tile, preferred_element_type=jnp.float32)
            * score_scale
        )
        exp_scores = jnp.where(visible, jnp.exp(scores), jnp.zeros_like(scores))
        weights = exp_scores / jnp.sum(exp_scores, axis=-1, keepdims=True)
        weights_reduced = weights.astype(jnp.bfloat16)
        attended = jnp.einsum(
            "grqk,gkd->grqd", weights_reduced, value_tile, preferred_element_type=jnp.float32
        )
        delta_col = jnp.sum(grad_tile.astype(jnp.float32) * attended, axis=-1, keepdims=True)
        prob_grad = jnp.einsum(
            "grqd,gkd->grqk", grad_tile, value_tile, preferred_element_type=jnp.float32
        )
        logit_gradient = (weights * (prob_grad - delta_col) * score_scale).astype(jnp.bfloat16)
        query_parts.append(
            jnp.einsum(
                "grqk,gkd->grqd", logit_gradient, key_tile, preferred_element_type=jnp.float32
            )
        )
        key_acc = key_acc.at[:, key_first:stop].add(
            jnp.einsum(
                "grqk,grqd->gkd", logit_gradient, query_tile, preferred_element_type=jnp.float32
            )
        )
        value_acc = value_acc.at[:, key_first:stop].add(
            jnp.einsum(
                "grqk,grqd->gkd", weights_reduced, grad_tile, preferred_element_type=jnp.float32
            )
        )
    query_normed_grad = jnp.transpose(jnp.concatenate(query_parts, axis=2), (2, 0, 1, 3))
    key_normed_grad = jnp.transpose(key_acc, (1, 0, 2))
    value_rows = jnp.transpose(value_acc, (1, 0, 2))
    query_grad = (
        norm_back(query_normed_grad, query_unit, query_inverse, query_scale)
        .astype(jnp.bfloat16)
        .reshape(total, groups * ratio * head_dim)
    )
    key_grad = (
        norm_back(key_normed_grad, key_unit, key_inverse, key_scale)
        .astype(jnp.bfloat16)
        .reshape(total, groups * head_dim)
    )
    value_grad = value_rows.astype(jnp.bfloat16).reshape(total, groups * head_dim)
    query_term = jnp.sum(query_normed_grad * query_unit, axis=(0, 1, 2))
    key_term = jnp.sum(key_normed_grad * key_unit, axis=(0, 1))
    both = summed_over(jnp.stack([query_term, key_term]), ("seq", "dp"))
    query_sum, key_sum = both[0], both[1]
    query_back, key_back, value_back = (
        lax.all_to_all(query_grad, "seq", split_axis=0, concat_axis=1, tiled=True),
        lax.all_to_all(key_grad, "seq", split_axis=0, concat_axis=1, tiled=True),
        lax.all_to_all(value_grad, "seq", split_axis=0, concat_axis=1, tiled=True),
    )
    return (
        query_back.reshape(1, 1, local_tokens, query_width),
        key_back.reshape(1, 1, local_tokens, key_width),
        value_back.reshape(1, 1, local_tokens, key_width),
        query_sum.reshape(1, head_dim),
        key_sum.reshape(1, head_dim),
    )


def solution(mesh):
    return jax.shard_map(
        on_device,
        mesh=mesh,
        in_specs=(
            P("pipe", "dp", "seq", None),
            P("pipe", "dp", "seq", None),
            P("pipe", "dp", "seq", None),
            P("pipe", "dp", "seq", None),
            P("pipe", "dp", None),
            P("pipe", None),
            P("pipe", None),
        ),
        out_specs=(
            P("pipe", "dp", "seq", None),
            P("pipe", "dp", "seq", None),
            P("pipe", "dp", "seq", None),
            P("pipe", None),
            P("pipe", None),
        ),
        check_vma=False,
    )
```

```python
import functools

import jax
import jax.numpy as jnp
from jax import lax
from jax.experimental import pallas as pl
from jax.experimental.pallas import tpu as pltpu
from jax.sharding import PartitionSpec as P

epsilon = 1e-06
score_scale = 168.0 ** (-0.5)


def summed_over(x, axes):
    devices = 1
    for axis in axes:
        devices *= lax.axis_size(axis)
    copies = jnp.broadcast_to(x[None], (devices,) + x.shape)
    return jnp.sum(lax.all_to_all(copies, axes, 0, 0, tiled=True), axis=0)


def shifted(x, axis, by):
    devices = lax.axis_size(axis)
    pairs = [(i, i + by) for i in range(devices) if 0 <= i + by < devices]
    return lax.ppermute(x, axis, pairs)


def normalize(values, gain):
    inverse = lax.rsqrt(jnp.mean(values * values, axis=-1, keepdims=True) + epsilon)
    unit = values * inverse
    return (unit, inverse, (unit * gain).astype(jnp.bfloat16))


def norm_back(grad_normed, unit, inverse, gain):
    grad_unit = grad_normed * gain
    centered = grad_unit - unit * jnp.mean(grad_unit * unit, axis=-1, keepdims=True)
    return inverse * centered


def window_kernel(ratio, head_dim, lo_ref, q_ref, k_ref, v_ref, up_ref, dq_ref, dk_ref, dv_ref):
    rows = q_ref.shape[0]
    keys = k_ref.shape[0]
    keys_f = k_ref[...]
    values = v_ref[...]
    col = lax.broadcasted_iota(jnp.int32, (rows, keys), 1)
    row = lax.broadcasted_iota(jnp.int32, (rows, keys), 0)
    visible = (col >= lo_ref[...]) & (col <= row + (keys - rows))
    dk = jnp.zeros((keys, head_dim), jnp.float32)
    dv = jnp.zeros((keys, head_dim), jnp.float32)
    for h in range(ratio):
        cols = slice(h * head_dim, (h + 1) * head_dim)
        q = q_ref[:, cols]
        up = up_ref[:, cols]
        scores = lax.dot_general(q, keys_f, (((1,), (1,)), ((), ())), preferred_element_type=jnp.float32) * score_scale
        exp_scores = jnp.where(visible, jnp.exp(scores), 0.0)
        weights = exp_scores / jnp.sum(exp_scores, axis=-1, keepdims=True)
        weights_low = weights.astype(jnp.bfloat16)
        attended = jnp.dot(weights_low, values, preferred_element_type=jnp.float32)
        delta = jnp.sum(up.astype(jnp.float32) * attended, axis=-1, keepdims=True)
        prob_grad = lax.dot_general(up, values, (((1,), (1,)), ((), ())), preferred_element_type=jnp.float32)
        score_grad = weights * (prob_grad - delta) * score_scale
        dq_ref[:, cols] = jnp.dot(score_grad.astype(jnp.bfloat16), keys_f, preferred_element_type=jnp.float32)
        dk = dk + jnp.dot(score_grad.T.astype(jnp.bfloat16), q, preferred_element_type=jnp.float32)
        dv = dv + jnp.dot(weights.T.astype(jnp.bfloat16), up, preferred_element_type=jnp.float32)
    dk_ref[...] = dk
    dv_ref[...] = dv


def window_attention(lo_rel, query_normed, key_cat, value_cat, upstream, ratio, head_dim):
    rows, query_width = query_normed.shape
    keys, key_width = key_cat.shape
    groups = key_width // head_dim
    qw = ratio * head_dim
    flops = 12 * rows * keys * head_dim * ratio * groups
    return pl.pallas_call(
        functools.partial(window_kernel, ratio, head_dim),
        grid=(groups,),
        in_specs=[
            pl.BlockSpec((rows, 1), lambda g: (0, 0)),
            pl.BlockSpec((rows, qw), lambda g: (0, g)),
            pl.BlockSpec((keys, head_dim), lambda g: (0, g)),
            pl.BlockSpec((keys, head_dim), lambda g: (0, g)),
            pl.BlockSpec((rows, qw), lambda g: (0, g)),
        ],
        out_specs=[
            pl.BlockSpec((rows, qw), lambda g: (0, g)),
            pl.BlockSpec((keys, head_dim), lambda g: (0, g)),
            pl.BlockSpec((keys, head_dim), lambda g: (0, g)),
        ],
        out_shape=[
            jax.ShapeDtypeStruct((rows, query_width), jnp.float32),
            jax.ShapeDtypeStruct((keys, key_width), jnp.float32),
            jax.ShapeDtypeStruct((keys, key_width), jnp.float32),
        ],
        cost_estimate=pl.CostEstimate(
            flops=flops,
            transcendentals=rows * keys * ratio * groups,
            bytes_accessed=2 * (2 * rows * query_width + 2 * keys * key_width) + 4 * (rows * query_width + 2 * keys * key_width),
        ),
    )(lo_rel, query_normed, key_cat, value_cat, upstream)


def on_device(query_proj, key_proj, value_proj, out_grad, lowest_key_index, query_gain, key_gain):
    rows = query_proj.shape[2]
    query_width = query_proj.shape[3]
    key_width = key_proj.shape[3]
    head_dim = query_gain.shape[1]
    groups = key_width // head_dim
    heads = query_width // head_dim
    ratio = heads // groups
    query_local = query_proj.reshape(rows, query_width)
    key_local = key_proj.reshape(rows, key_width)
    value_local = value_proj.reshape(rows, key_width)
    pipe_devices = lax.axis_size("pipe")
    upstream = lax.ppermute(
        out_grad.reshape(rows, query_width), "pipe", [(i, (i - 1) % pipe_devices) for i in range(pipe_devices)]
    )
    halo = shifted(jnp.stack([key_local, value_local]), "seq", 1)
    query_scale = query_gain.reshape(head_dim)
    key_scale = key_gain.reshape(head_dim)
    query_unit, query_inverse, query_normed = normalize(
        query_local.astype(jnp.float32).reshape(rows, heads, head_dim), query_scale
    )
    key_unit, key_inverse, key_normed = normalize(
        key_local.astype(jnp.float32).reshape(rows, groups, head_dim), key_scale
    )
    prev_unit, _, prev_normed = normalize(halo[0].astype(jnp.float32).reshape(rows, groups, head_dim), key_scale)
    key_cat = jnp.concatenate([prev_normed.reshape(rows, key_width), key_normed.reshape(rows, key_width)], axis=0)
    value_cat = jnp.concatenate([halo[1], value_local], axis=0)
    block = lax.axis_index("seq")
    first = block * rows
    lo_rel = (lax.dynamic_slice(lowest_key_index.reshape(-1), (first,), (rows,)) - (first - rows)).reshape(rows, 1)
    query_normed_grad, key_parts, value_parts = window_attention(
        lo_rel, query_normed.reshape(rows, query_width), key_cat, value_cat, upstream, ratio, head_dim
    )
    back = shifted(jnp.stack([key_parts[:rows], value_parts[:rows]]), "seq", -1)
    key_normed_grad = (key_parts[rows:] + back[0]).reshape(rows, groups, head_dim)
    value_rows = value_parts[rows:] + back[1]
    query_normed_grad = query_normed_grad.reshape(rows, heads, head_dim)
    query_term = jnp.sum(query_normed_grad * query_unit, axis=(0, 1))
    key_term = jnp.sum(key_parts[rows:].reshape(rows, groups, head_dim) * key_unit, axis=(0, 1)) + jnp.sum(
        key_parts[:rows].reshape(rows, groups, head_dim) * prev_unit, axis=(0, 1)
    )
    both = summed_over(jnp.stack([query_term, key_term]), ("dp", "seq"))
    query_grad = norm_back(query_normed_grad, query_unit, query_inverse, query_scale).astype(jnp.bfloat16)
    key_grad = norm_back(key_normed_grad, key_unit, key_inverse, key_scale).astype(jnp.bfloat16)
    value_grad = value_rows.astype(jnp.bfloat16)
    return (
        query_grad.reshape(1, 1, rows, query_width),
        key_grad.reshape(1, 1, rows, key_width),
        value_grad.reshape(1, 1, rows, key_width),
        both[0].reshape(1, head_dim),
        both[1].reshape(1, head_dim),
    )


def solution(mesh):
    return jax.shard_map(
        on_device,
        mesh=mesh,
        in_specs=(
            P("pipe", "dp", "seq", None),
            P("pipe", "dp", "seq", None),
            P("pipe", "dp", "seq", None),
            P("pipe", "dp", "seq", None),
            P("pipe", "dp", None),
            P("pipe", None),
            P("pipe", None),
        ),
        out_specs=(
            P("pipe", "dp", "seq", None),
            P("pipe", "dp", "seq", None),
            P("pipe", "dp", "seq", None),
            P("pipe", None),
            P("pipe", None),
        ),
        check_vma=False,
    )
```

```python
import functools

import jax
import jax.numpy as jnp
from jax import lax
from jax.experimental import pallas as pl
from jax.sharding import PartitionSpec as P

epsilon = 1e-06
score_scale = 168.0 ** (-0.5)


def summed_over(x, axes):
    devices = 1
    for axis in axes:
        devices *= lax.axis_size(axis)
    copies = jnp.broadcast_to(x[None], (devices,) + x.shape)
    return jnp.sum(lax.all_to_all(copies, axes, 0, 0, tiled=True), axis=0)


def shifted(x, axis, by):
    devices = lax.axis_size(axis)
    pairs = [(i, i + by) for i in range(devices) if 0 <= i + by < devices]
    return lax.ppermute(x, axis, pairs)


def normalize(values, gain):
    inverse = lax.rsqrt(jnp.mean(values * values, axis=-1, keepdims=True) + epsilon)
    unit = values * inverse
    return (unit, inverse, (unit * gain).astype(jnp.bfloat16))


def norm_back(grad_normed, unit, inverse, gain):
    grad_unit = grad_normed * gain
    centered = grad_unit - unit * jnp.mean(grad_unit * unit, axis=-1, keepdims=True)
    return inverse * centered


def window_kernel(ratio, head_dim, lo_ref, qgain_ref, kgain_ref, q_ref, k_ref, v_ref, halo_ref, up_ref,
                  qgrad_ref, own_ref, send_ref, gains_ref):
    rows = q_ref.shape[0]
    qgain = qgain_ref[...]
    kgain = kgain_ref[...]
    key_raw = jnp.concatenate([halo_ref[0], k_ref[...]], axis=0).astype(jnp.float32)
    values = jnp.concatenate([halo_ref[1], v_ref[...]], axis=0)
    keys = key_raw.shape[0]
    key_unit, _, key_normed = normalize(key_raw, kgain)
    col = lax.broadcasted_iota(jnp.int32, (rows, keys), 1)
    row = lax.broadcasted_iota(jnp.int32, (rows, keys), 0)
    visible = (col >= lo_ref[...]) & (col <= row + (keys - rows))
    dk = jnp.zeros((keys, head_dim), jnp.float32)
    dv = jnp.zeros((keys, head_dim), jnp.float32)
    qterm = jnp.zeros((1, head_dim), jnp.float32)
    for h in range(ratio):
        cols = slice(h * head_dim, (h + 1) * head_dim)
        query_unit, query_inverse, q = normalize(q_ref[:, cols].astype(jnp.float32), qgain)
        up = up_ref[:, cols]
        scores = lax.dot_general(q, key_normed, (((1,), (1,)), ((), ())), preferred_element_type=jnp.float32) * score_scale
        exp_scores = jnp.where(visible, jnp.exp(scores), 0.0)
        weights = exp_scores / jnp.sum(exp_scores, axis=-1, keepdims=True)
        weights_low = weights.astype(jnp.bfloat16)
        attended = jnp.dot(weights_low, values, preferred_element_type=jnp.float32)
        delta = jnp.sum(up.astype(jnp.float32) * attended, axis=-1, keepdims=True)
        prob_grad = lax.dot_general(up, values, (((1,), (1,)), ((), ())), preferred_element_type=jnp.float32)
        score_grad = weights * (prob_grad - delta) * score_scale
        dq = jnp.dot(score_grad.astype(jnp.bfloat16), key_normed, preferred_element_type=jnp.float32)
        qgrad_ref[:, cols] = norm_back(dq, query_unit, query_inverse, qgain).astype(qgrad_ref.dtype)
        qterm = qterm + jnp.sum(dq * query_unit, axis=0, keepdims=True)
        dk = dk + jnp.dot(score_grad.T.astype(jnp.bfloat16), q, preferred_element_type=jnp.float32)
        dv = dv + jnp.dot(weights.T.astype(jnp.bfloat16), up, preferred_element_type=jnp.float32)
    kterm = jnp.sum(dk * key_unit, axis=0, keepdims=True)
    own_ref[0] = dk[rows:]
    own_ref[1] = dv[rows:]
    send_ref[0] = dk[:rows].astype(send_ref.dtype)
    send_ref[1] = dv[:rows].astype(send_ref.dtype)

    @pl.when(pl.program_id(0) == 0)
    def _():
        gains_ref[...] = jnp.zeros_like(gains_ref)

    gains_ref[...] += jnp.concatenate([qterm, kterm], axis=0)


def window_attention(lo_rel, query_gain, key_gain, query_local, key_local, value_local, halo, upstream, ratio, head_dim):
    rows, query_width = query_local.shape
    key_width = key_local.shape[1]
    groups = key_width // head_dim
    qw = ratio * head_dim
    keys = 2 * rows
    flops = 12 * rows * keys * head_dim * ratio * groups
    return pl.pallas_call(
        functools.partial(window_kernel, ratio, head_dim),
        grid=(groups,),
        in_specs=[
            pl.BlockSpec((rows, 1), lambda g: (0, 0)),
            pl.BlockSpec((1, head_dim), lambda g: (0, 0)),
            pl.BlockSpec((1, head_dim), lambda g: (0, 0)),
            pl.BlockSpec((rows, qw), lambda g: (0, g)),
            pl.BlockSpec((rows, head_dim), lambda g: (0, g)),
            pl.BlockSpec((rows, head_dim), lambda g: (0, g)),
            pl.BlockSpec((2, rows, head_dim), lambda g: (0, 0, g)),
            pl.BlockSpec((rows, qw), lambda g: (0, g)),
        ],
        out_specs=[
            pl.BlockSpec((rows, qw), lambda g: (0, g)),
            pl.BlockSpec((2, rows, head_dim), lambda g: (0, 0, g)),
            pl.BlockSpec((2, rows, head_dim), lambda g: (0, 0, g)),
            pl.BlockSpec((2, head_dim), lambda g: (0, 0)),
        ],
        out_shape=[
            jax.ShapeDtypeStruct((rows, query_width), jnp.bfloat16),
            jax.ShapeDtypeStruct((2, rows, key_width), jnp.float32),
            jax.ShapeDtypeStruct((2, rows, key_width), jnp.bfloat16),
            jax.ShapeDtypeStruct((2, head_dim), jnp.float32),
        ],
        cost_estimate=pl.CostEstimate(
            flops=flops,
            transcendentals=rows * keys * ratio * groups,
            bytes_accessed=2 * (4 * rows * query_width + 6 * rows * key_width) + 8 * rows * key_width,
        ),
    )(lo_rel, query_gain, key_gain, query_local, key_local, value_local, halo, upstream)


def on_device(query_proj, key_proj, value_proj, out_grad, lowest_key_index, query_gain, key_gain):
    rows = query_proj.shape[2]
    query_width = query_proj.shape[3]
    key_width = key_proj.shape[3]
    head_dim = query_gain.shape[1]
    groups = key_width // head_dim
    heads = query_width // head_dim
    ratio = heads // groups
    query_local = query_proj.reshape(rows, query_width)
    key_local = key_proj.reshape(rows, key_width)
    value_local = value_proj.reshape(rows, key_width)
    pipe_devices = lax.axis_size("pipe")
    upstream = lax.ppermute(
        out_grad.reshape(rows, query_width), "pipe", [(i, (i - 1) % pipe_devices) for i in range(pipe_devices)]
    )
    halo = shifted(jnp.stack([key_local, value_local]), "seq", 1)
    block = lax.axis_index("seq")
    first = block * rows
    lo_rel = (lax.dynamic_slice(lowest_key_index.reshape(-1), (first,), (rows,)) - (first - rows)).reshape(rows, 1)
    query_grad, own, send, gain_terms = window_attention(
        lo_rel, query_gain, key_gain, query_local, key_local, value_local, halo, upstream, ratio, head_dim
    )
    back = shifted(send, "seq", -1)
    both = summed_over(gain_terms, ("dp", "seq"))
    key_scale = key_gain.reshape(head_dim)
    key_unit, key_inverse, _ = normalize(key_local.astype(jnp.float32).reshape(rows, groups, head_dim), key_scale)
    key_normed_grad = (own[0] + back[0].astype(jnp.float32)).reshape(rows, groups, head_dim)
    value_rows = own[1] + back[1].astype(jnp.float32)
    key_grad = norm_back(key_normed_grad, key_unit, key_inverse, key_scale).astype(jnp.bfloat16)
    value_grad = value_rows.astype(jnp.bfloat16)
    return (
        query_grad.reshape(1, 1, rows, query_width),
        key_grad.reshape(1, 1, rows, key_width),
        value_grad.reshape(1, 1, rows, key_width),
        both[0].reshape(1, head_dim),
        both[1].reshape(1, head_dim),
    )


def solution(mesh):
    return jax.shard_map(
        on_device,
        mesh=mesh,
        in_specs=(
            P("pipe", "dp", "seq", None),
            P("pipe", "dp", "seq", None),
            P("pipe", "dp", "seq", None),
            P("pipe", "dp", "seq", None),
            P("pipe", "dp", None),
            P("pipe", None),
            P("pipe", None),
        ),
        out_specs=(
            P("pipe", "dp", "seq", None),
            P("pipe", "dp", "seq", None),
            P("pipe", "dp", "seq", None),
            P("pipe", None),
            P("pipe", None),
        ),
        check_vma=False,
    )
```

```python
import functools

import jax
import jax.numpy as jnp
from jax import lax
from jax.experimental import pallas as pl
from jax.sharding import PartitionSpec as P

epsilon = 1e-06
score_scale = 168.0 ** (-0.5)


def summed_over(x, axes):
    devices = 1
    for axis in axes:
        devices *= lax.axis_size(axis)
    copies = jnp.broadcast_to(x[None], (devices,) + x.shape)
    return jnp.sum(lax.all_to_all(copies, axes, 0, 0, tiled=True), axis=0)


def shifted(x, axis, by):
    devices = lax.axis_size(axis)
    pairs = [(i, i + by) for i in range(devices) if 0 <= i + by < devices]
    return lax.ppermute(x, axis, pairs)


def normalize(values, gain):
    inverse = lax.rsqrt(jnp.mean(values * values, axis=-1, keepdims=True) + epsilon)
    unit = values * inverse
    return (unit, inverse, (unit * gain).astype(jnp.bfloat16))


def norm_back(grad_normed, unit, inverse, gain):
    grad_unit = grad_normed * gain
    centered = grad_unit - unit * jnp.mean(grad_unit * unit, axis=-1, keepdims=True)
    return inverse * centered


def window_kernel(ratio, head_dim, per_step, lo_ref, qgain_ref, kgain_ref, q_ref, k_ref, v_ref, halo_ref, up_ref,
                  qgrad_ref, own_ref, send_ref, gains_ref):
    @pl.when(pl.program_id(0) == 0)
    def _():
        gains_ref[...] = jnp.zeros_like(gains_ref)

    for g in range(per_step):
        one_group(ratio, head_dim, g, lo_ref, qgain_ref, kgain_ref, q_ref, k_ref, v_ref, halo_ref, up_ref,
                  qgrad_ref, own_ref, send_ref, gains_ref)


def one_group(ratio, head_dim, g, lo_ref, qgain_ref, kgain_ref, q_ref, k_ref, v_ref, halo_ref, up_ref,
              qgrad_ref, own_ref, send_ref, gains_ref):
    rows = q_ref.shape[0]
    qgain = qgain_ref[...]
    kgain = kgain_ref[...]
    kc = slice(g * head_dim, (g + 1) * head_dim)
    key_raw = jnp.concatenate([halo_ref[0, :, kc], k_ref[:, kc]], axis=0).astype(jnp.float32)
    values = jnp.concatenate([halo_ref[1, :, kc], v_ref[:, kc]], axis=0)
    keys = key_raw.shape[0]
    key_unit, _, key_normed = normalize(key_raw, kgain)
    heads = [slice((g * ratio + h) * head_dim, (g * ratio + h + 1) * head_dim) for h in range(ratio)]
    query_unit, query_inverse, q = normalize(
        jnp.concatenate([q_ref[:, c] for c in heads], axis=0).astype(jnp.float32), qgain
    )
    up = jnp.concatenate([up_ref[:, c] for c in heads], axis=0)
    stacked = ratio * rows
    col = lax.broadcasted_iota(jnp.int32, (stacked, keys), 1)
    row = lax.broadcasted_iota(jnp.int32, (stacked, keys), 0) % rows
    lo = jnp.concatenate([lo_ref[...]] * ratio, axis=0)
    visible = (col >= lo) & (col <= row + (keys - rows))
    scores = lax.dot_general(q, key_normed, (((1,), (1,)), ((), ())), preferred_element_type=jnp.float32) * score_scale
    exp_scores = jnp.where(visible, jnp.exp(scores), 0.0)
    weights = exp_scores / jnp.sum(exp_scores, axis=-1, keepdims=True)
    weights_low = weights.astype(jnp.bfloat16)
    attended = jnp.dot(weights_low, values, preferred_element_type=jnp.float32)
    delta = jnp.sum(up.astype(jnp.float32) * attended, axis=-1, keepdims=True)
    prob_grad = lax.dot_general(up, values, (((1,), (1,)), ((), ())), preferred_element_type=jnp.float32)
    score_grad = weights * (prob_grad - delta) * score_scale
    dq = jnp.dot(score_grad.astype(jnp.bfloat16), key_normed, preferred_element_type=jnp.float32)
    query_grad = norm_back(dq, query_unit, query_inverse, qgain).astype(qgrad_ref.dtype)
    for h, c in enumerate(heads):
        qgrad_ref[:, c] = query_grad[h * rows:(h + 1) * rows]
    qterm = jnp.sum(dq * query_unit, axis=0, keepdims=True)
    dk = jnp.dot(score_grad.T.astype(jnp.bfloat16), q, preferred_element_type=jnp.float32)
    dv = jnp.dot(weights.T.astype(jnp.bfloat16), up, preferred_element_type=jnp.float32)
    kterm = jnp.sum(dk * key_unit, axis=0, keepdims=True)
    own_ref[0, :, kc] = dk[rows:]
    own_ref[1, :, kc] = dv[rows:]
    send_ref[0, :, kc] = dk[:rows].astype(send_ref.dtype)
    send_ref[1, :, kc] = dv[:rows].astype(send_ref.dtype)
    gains_ref[...] += jnp.concatenate([qterm, kterm], axis=0)


GROUPS_PER_STEP = 1


def window_attention(lo_rel, query_gain, key_gain, query_local, key_local, value_local, halo, upstream, ratio, head_dim):
    rows, query_width = query_local.shape
    key_width = key_local.shape[1]
    per_step = GROUPS_PER_STEP
    groups = key_width // (head_dim * per_step)
    kw = head_dim * per_step
    qw = ratio * kw
    keys = 2 * rows
    flops = 12 * rows * keys * head_dim * ratio * groups * per_step
    return pl.pallas_call(
        functools.partial(window_kernel, ratio, head_dim, per_step),
        grid=(groups,),
        in_specs=[
            pl.BlockSpec((rows, 1), lambda g: (0, 0)),
            pl.BlockSpec((1, head_dim), lambda g: (0, 0)),
            pl.BlockSpec((1, head_dim), lambda g: (0, 0)),
            pl.BlockSpec((rows, qw), lambda g: (0, g)),
            pl.BlockSpec((rows, kw), lambda g: (0, g)),
            pl.BlockSpec((rows, kw), lambda g: (0, g)),
            pl.BlockSpec((2, rows, kw), lambda g: (0, 0, g)),
            pl.BlockSpec((rows, qw), lambda g: (0, g)),
        ],
        out_specs=[
            pl.BlockSpec((rows, qw), lambda g: (0, g)),
            pl.BlockSpec((2, rows, kw), lambda g: (0, 0, g)),
            pl.BlockSpec((2, rows, kw), lambda g: (0, 0, g)),
            pl.BlockSpec((2, head_dim), lambda g: (0, 0)),
        ],
        out_shape=[
            jax.ShapeDtypeStruct((rows, query_width), jnp.bfloat16),
            jax.ShapeDtypeStruct((2, rows, key_width), jnp.float32),
            jax.ShapeDtypeStruct((2, rows, key_width), jnp.bfloat16),
            jax.ShapeDtypeStruct((2, head_dim), jnp.float32),
        ],
        cost_estimate=pl.CostEstimate(
            flops=flops,
            transcendentals=rows * keys * ratio * groups * per_step,
            bytes_accessed=2 * (4 * rows * query_width + 6 * rows * key_width) + 8 * rows * key_width,
        ),
    )(lo_rel, query_gain, key_gain, query_local, key_local, value_local, halo, upstream)


def on_device(query_proj, key_proj, value_proj, out_grad, lowest_key_index, query_gain, key_gain):
    rows = query_proj.shape[2]
    query_width = query_proj.shape[3]
    key_width = key_proj.shape[3]
    head_dim = query_gain.shape[1]
    groups = key_width // head_dim
    heads = query_width // head_dim
    ratio = heads // groups
    query_local = query_proj.reshape(rows, query_width)
    key_local = key_proj.reshape(rows, key_width)
    value_local = value_proj.reshape(rows, key_width)
    pipe_devices = lax.axis_size("pipe")
    upstream = lax.ppermute(
        out_grad.reshape(rows, query_width), "pipe", [(i, (i - 1) % pipe_devices) for i in range(pipe_devices)]
    )
    halo = shifted(jnp.stack([key_local, value_local]), "seq", 1)
    block = lax.axis_index("seq")
    first = block * rows
    lo_rel = (lax.dynamic_slice(lowest_key_index.reshape(-1), (first,), (rows,)) - (first - rows)).reshape(rows, 1)
    query_grad, own, send, gain_terms = window_attention(
        lo_rel, query_gain, key_gain, query_local, key_local, value_local, halo, upstream, ratio, head_dim
    )
    back = shifted(send, "seq", -1)
    both = summed_over(gain_terms, ("dp", "seq"))
    key_scale = key_gain.reshape(head_dim)
    key_unit, key_inverse, _ = normalize(key_local.astype(jnp.float32).reshape(rows, groups, head_dim), key_scale)
    key_normed_grad = (own[0] + back[0].astype(jnp.float32)).reshape(rows, groups, head_dim)
    value_rows = own[1] + back[1].astype(jnp.float32)
    key_grad = norm_back(key_normed_grad, key_unit, key_inverse, key_scale).astype(jnp.bfloat16)
    value_grad = value_rows.astype(jnp.bfloat16)
    return (
        query_grad.reshape(1, 1, rows, query_width),
        key_grad.reshape(1, 1, rows, key_width),
        value_grad.reshape(1, 1, rows, key_width),
        both[0].reshape(1, head_dim),
        both[1].reshape(1, head_dim),
    )


def solution(mesh):
    return jax.shard_map(
        on_device,
        mesh=mesh,
        in_specs=(
            P("pipe", "dp", "seq", None),
            P("pipe", "dp", "seq", None),
            P("pipe", "dp", "seq", None),
            P("pipe", "dp", "seq", None),
            P("pipe", "dp", None),
            P("pipe", None),
            P("pipe", None),
        ),
        out_specs=(
            P("pipe", "dp", "seq", None),
            P("pipe", "dp", "seq", None),
            P("pipe", "dp", "seq", None),
            P("pipe", None),
            P("pipe", None),
        ),
        check_vma=False,
    )
```

```python
import functools

import jax
import jax.numpy as jnp
from jax import lax
from jax.experimental import pallas as pl
from jax.sharding import PartitionSpec as P

epsilon = 1e-06
score_scale = 168.0 ** (-0.5)


def gathered_over(x, axes):
    devices = 1
    for axis in axes:
        devices *= lax.axis_size(axis)
    copies = jnp.broadcast_to(x[None], (devices,) + x.shape)
    return lax.all_to_all(copies, axes, 0, 0, tiled=True)


def shifted(x, axis, by):
    devices = lax.axis_size(axis)
    pairs = [(i, i + by) for i in range(devices) if 0 <= i + by < devices]
    return lax.ppermute(x, axis, pairs)


def normalize(values, gain):
    inverse = lax.rsqrt(jnp.mean(values * values, axis=-1, keepdims=True) + epsilon)
    unit = values * inverse
    return (unit, inverse, (unit * gain).astype(jnp.bfloat16))


def norm_back(grad_normed, unit, inverse, gain):
    grad_unit = grad_normed * gain
    centered = grad_unit - unit * jnp.mean(grad_unit * unit, axis=-1, keepdims=True)
    return inverse * centered


def window_kernel(ratio, head_dim, per_step, lo_ref, qgain_ref, kgain_ref, q_ref, k_ref, v_ref, halo_ref, up_ref,
                  qgrad_ref, own_ref, send_ref, gains_ref):
    @pl.when(pl.program_id(0) == 0)
    def _():
        gains_ref[...] = jnp.zeros_like(gains_ref)

    for g in range(per_step):
        one_group(ratio, head_dim, g, lo_ref, qgain_ref, kgain_ref, q_ref, k_ref, v_ref, halo_ref, up_ref,
                  qgrad_ref, own_ref, send_ref, gains_ref)


def one_group(ratio, head_dim, g, lo_ref, qgain_ref, kgain_ref, q_ref, k_ref, v_ref, halo_ref, up_ref,
              qgrad_ref, own_ref, send_ref, gains_ref):
    rows = q_ref.shape[0]
    qgain = qgain_ref[...]
    kgain = kgain_ref[...]
    kc = slice(g * head_dim, (g + 1) * head_dim)
    key_raw = jnp.concatenate([halo_ref[0, :, kc], k_ref[:, kc]], axis=0).astype(jnp.float32)
    values = jnp.concatenate([halo_ref[1, :, kc], v_ref[:, kc]], axis=0)
    keys = key_raw.shape[0]
    key_unit, _, key_normed = normalize(key_raw, kgain)
    heads = [slice((g * ratio + h) * head_dim, (g * ratio + h + 1) * head_dim) for h in range(ratio)]
    query_unit, query_inverse, q = normalize(
        jnp.concatenate([q_ref[:, c] for c in heads], axis=0).astype(jnp.float32), qgain
    )
    up = jnp.concatenate([up_ref[:, c] for c in heads], axis=0)
    stacked = ratio * rows
    col = lax.broadcasted_iota(jnp.int32, (stacked, keys), 1)
    row = lax.broadcasted_iota(jnp.int32, (stacked, keys), 0) % rows
    lo = jnp.concatenate([lo_ref[...]] * ratio, axis=0)
    visible = (col >= lo) & (col <= row + (keys - rows))
    scores = lax.dot_general(q, key_normed, (((1,), (1,)), ((), ())), preferred_element_type=jnp.float32) * score_scale
    exp_scores = jnp.where(visible, jnp.exp(scores), 0.0)
    weights = exp_scores / jnp.sum(exp_scores, axis=-1, keepdims=True)
    weights_low = weights.astype(jnp.bfloat16)
    attended = jnp.dot(weights_low, values, preferred_element_type=jnp.float32)
    delta = jnp.sum(up.astype(jnp.float32) * attended, axis=-1, keepdims=True)
    prob_grad = lax.dot_general(up, values, (((1,), (1,)), ((), ())), preferred_element_type=jnp.float32)
    score_grad = weights * (prob_grad - delta) * score_scale
    dq = jnp.dot(score_grad.astype(jnp.bfloat16), key_normed, preferred_element_type=jnp.float32)
    query_grad = norm_back(dq, query_unit, query_inverse, qgain).astype(qgrad_ref.dtype)
    for h, c in enumerate(heads):
        qgrad_ref[:, c] = query_grad[h * rows:(h + 1) * rows]
    qterm = jnp.sum(dq * query_unit, axis=0, keepdims=True)
    dk = jnp.dot(score_grad.T.astype(jnp.bfloat16), q, preferred_element_type=jnp.float32)
    dv = jnp.dot(weights.T.astype(jnp.bfloat16), up, preferred_element_type=jnp.float32)
    kterm = jnp.sum(dk * key_unit, axis=0, keepdims=True)
    own_ref[0, :, kc] = dk[rows:]
    own_ref[1, :, kc] = dv[rows:]
    send_ref[0, :, kc] = dk[:rows].astype(send_ref.dtype)
    send_ref[1, :, kc] = dv[:rows].astype(send_ref.dtype)
    gains_ref[...] += jnp.concatenate([qterm, kterm], axis=0)


GROUPS_PER_STEP = 1


def window_attention(lo_rel, query_gain, key_gain, query_local, key_local, value_local, halo, upstream, ratio, head_dim):
    rows, query_width = query_local.shape
    key_width = key_local.shape[1]
    per_step = GROUPS_PER_STEP
    groups = key_width // (head_dim * per_step)
    kw = head_dim * per_step
    qw = ratio * kw
    keys = 2 * rows
    flops = 12 * rows * keys * head_dim * ratio * groups * per_step
    return pl.pallas_call(
        functools.partial(window_kernel, ratio, head_dim, per_step),
        grid=(groups,),
        in_specs=[
            pl.BlockSpec((rows, 1), lambda g: (0, 0)),
            pl.BlockSpec((1, head_dim), lambda g: (0, 0)),
            pl.BlockSpec((1, head_dim), lambda g: (0, 0)),
            pl.BlockSpec((rows, qw), lambda g: (0, g)),
            pl.BlockSpec((rows, kw), lambda g: (0, g)),
            pl.BlockSpec((rows, kw), lambda g: (0, g)),
            pl.BlockSpec((2, rows, kw), lambda g: (0, 0, g)),
            pl.BlockSpec((rows, qw), lambda g: (0, g)),
        ],
        out_specs=[
            pl.BlockSpec((rows, qw), lambda g: (0, g)),
            pl.BlockSpec((2, rows, kw), lambda g: (0, 0, g)),
            pl.BlockSpec((2, rows, kw), lambda g: (0, 0, g)),
            pl.BlockSpec((2, head_dim), lambda g: (0, 0)),
        ],
        out_shape=[
            jax.ShapeDtypeStruct((rows, query_width), jnp.bfloat16),
            jax.ShapeDtypeStruct((2, rows, key_width), jnp.float32),
            jax.ShapeDtypeStruct((2, rows, key_width), jnp.bfloat16),
            jax.ShapeDtypeStruct((2, head_dim), jnp.float32),
        ],
        cost_estimate=pl.CostEstimate(
            flops=flops,
            transcendentals=rows * keys * ratio * groups * per_step,
            bytes_accessed=2 * (4 * rows * query_width + 6 * rows * key_width) + 8 * rows * key_width,
        ),
    )(lo_rel, query_gain, key_gain, query_local, key_local, value_local, halo, upstream)


def on_device(query_proj, key_proj, value_proj, out_grad, lowest_key_index, query_gain, key_gain):
    rows = query_proj.shape[2]
    query_width = query_proj.shape[3]
    key_width = key_proj.shape[3]
    head_dim = query_gain.shape[1]
    groups = key_width // head_dim
    heads = query_width // head_dim
    ratio = heads // groups
    query_local = query_proj.reshape(rows, query_width)
    key_local = key_proj.reshape(rows, key_width)
    value_local = value_proj.reshape(rows, key_width)
    pipe_devices = lax.axis_size("pipe")
    upstream = lax.ppermute(
        out_grad.reshape(rows, query_width), "pipe", [(i, (i - 1) % pipe_devices) for i in range(pipe_devices)]
    )
    halo = shifted(jnp.stack([key_local, value_local]), "seq", 1)
    block = lax.axis_index("seq")
    first = block * rows
    lo_rel = (lax.dynamic_slice(lowest_key_index.reshape(-1), (first,), (rows,)) - (first - rows)).reshape(rows, 1)
    key_scale = key_gain.reshape(head_dim)
    key_unit, key_inverse, _ = normalize(key_local.astype(jnp.float32).reshape(rows, groups, head_dim), key_scale)
    key_unit, key_inverse, query_local = lax.optimization_barrier((key_unit, key_inverse, query_local))
    query_grad, own, send, gain_terms = window_attention(
        lo_rel, query_gain, key_gain, query_local, key_local, value_local, halo, upstream, ratio, head_dim
    )
    back = shifted(send, "seq", -1)
    received = gathered_over(gain_terms, ("dp", "seq"))
    key_normed_grad = (own[0] + back[0].astype(jnp.float32)).reshape(rows, groups, head_dim)
    value_rows = own[1] + back[1].astype(jnp.float32)
    key_grad = norm_back(key_normed_grad, key_unit, key_inverse, key_scale).astype(jnp.bfloat16)
    value_grad = value_rows.astype(jnp.bfloat16)
    key_grad, value_grad, received = lax.optimization_barrier((key_grad, value_grad, received))
    both = jnp.sum(received, axis=0)
    return (
        query_grad.reshape(1, 1, rows, query_width),
        key_grad.reshape(1, 1, rows, key_width),
        value_grad.reshape(1, 1, rows, key_width),
        both[0].reshape(1, head_dim),
        both[1].reshape(1, head_dim),
    )


def solution(mesh):
    return jax.shard_map(
        on_device,
        mesh=mesh,
        in_specs=(
            P("pipe", "dp", "seq", None),
            P("pipe", "dp", "seq", None),
            P("pipe", "dp", "seq", None),
            P("pipe", "dp", "seq", None),
            P("pipe", "dp", None),
            P("pipe", None),
            P("pipe", None),
        ),
        out_specs=(
            P("pipe", "dp", "seq", None),
            P("pipe", "dp", "seq", None),
            P("pipe", "dp", "seq", None),
            P("pipe", None),
            P("pipe", None),
        ),
        check_vma=False,
    )
```

```python
import functools

import jax
import jax.numpy as jnp
from jax import lax
from jax.experimental import pallas as pl
from jax.sharding import PartitionSpec as P

epsilon = 1e-06
score_scale = 168.0 ** (-0.5)


def gathered_over(x, axes):
    devices = 1
    for axis in axes:
        devices *= lax.axis_size(axis)
    copies = jnp.broadcast_to(x[None], (devices,) + x.shape)
    return lax.all_to_all(copies, axes, 0, 0, tiled=True)


def shifted(x, axis, by):
    devices = lax.axis_size(axis)
    pairs = [(i, i + by) for i in range(devices) if 0 <= i + by < devices]
    return lax.ppermute(x, axis, pairs)


def normalize(values, gain):
    inverse = lax.rsqrt(jnp.mean(values * values, axis=-1, keepdims=True) + epsilon)
    unit = values * inverse
    return (unit, inverse, (unit * gain).astype(jnp.bfloat16))


def norm_back(grad_normed, unit, inverse, gain):
    grad_unit = grad_normed * gain
    centered = grad_unit - unit * jnp.mean(grad_unit * unit, axis=-1, keepdims=True)
    return inverse * centered


def window_kernel(ratio, head_dim, per_step, lo_ref, qgain_ref, kgain_ref, q_ref, k_ref, v_ref, kh_ref, vh_ref,
                  up_ref, qgrad_ref, own_ref, send_ref, gains_ref):
    @pl.when(pl.program_id(0) == 0)
    def _():
        gains_ref[...] = jnp.zeros_like(gains_ref)

    for g in range(per_step):
        one_group(ratio, head_dim, g, lo_ref, qgain_ref, kgain_ref, q_ref, k_ref, v_ref, kh_ref, vh_ref, up_ref,
                  qgrad_ref, own_ref, send_ref, gains_ref)


def one_group(ratio, head_dim, g, lo_ref, qgain_ref, kgain_ref, q_ref, k_ref, v_ref, kh_ref, vh_ref, up_ref,
              qgrad_ref, own_ref, send_ref, gains_ref):
    rows = q_ref.shape[0]
    qgain = qgain_ref[...]
    kgain = kgain_ref[...]
    kc = slice(g * head_dim, (g + 1) * head_dim)
    key_raw = jnp.concatenate([kh_ref[:, kc], k_ref[:, kc]], axis=0).astype(jnp.float32)
    values = jnp.concatenate([vh_ref[:, kc], v_ref[:, kc]], axis=0)
    keys = key_raw.shape[0]
    key_unit, _, key_normed = normalize(key_raw, kgain)
    heads = [slice((g * ratio + h) * head_dim, (g * ratio + h + 1) * head_dim) for h in range(ratio)]
    query_unit, query_inverse, q = normalize(
        jnp.concatenate([q_ref[:, c] for c in heads], axis=0).astype(jnp.float32), qgain
    )
    up = jnp.concatenate([up_ref[:, c] for c in heads], axis=0)
    stacked = ratio * rows
    col = lax.broadcasted_iota(jnp.int32, (stacked, keys), 1)
    row = lax.broadcasted_iota(jnp.int32, (stacked, keys), 0) % rows
    lo = jnp.concatenate([lo_ref[...]] * ratio, axis=0)
    visible = (col >= lo) & (col <= row + (keys - rows))
    scores = lax.dot_general(q, key_normed, (((1,), (1,)), ((), ())), preferred_element_type=jnp.float32) * score_scale
    exp_scores = jnp.where(visible, jnp.exp(scores), 0.0)
    weights = exp_scores / jnp.sum(exp_scores, axis=-1, keepdims=True)
    weights_low = weights.astype(jnp.bfloat16)
    attended = jnp.dot(weights_low, values, preferred_element_type=jnp.float32)
    delta = jnp.sum(up.astype(jnp.float32) * attended, axis=-1, keepdims=True)
    prob_grad = lax.dot_general(up, values, (((1,), (1,)), ((), ())), preferred_element_type=jnp.float32)
    score_grad = weights * (prob_grad - delta) * score_scale
    dq = jnp.dot(score_grad.astype(jnp.bfloat16), key_normed, preferred_element_type=jnp.float32)
    query_grad = norm_back(dq, query_unit, query_inverse, qgain).astype(qgrad_ref.dtype)
    for h, c in enumerate(heads):
        qgrad_ref[:, c] = query_grad[h * rows:(h + 1) * rows]
    qterm = jnp.sum(dq * query_unit, axis=0, keepdims=True)
    dk = jnp.dot(score_grad.T.astype(jnp.bfloat16), q, preferred_element_type=jnp.float32)
    dv = jnp.dot(weights.T.astype(jnp.bfloat16), up, preferred_element_type=jnp.float32)
    kterm = jnp.sum(dk * key_unit, axis=0, keepdims=True)
    own_ref[0, :, kc] = dk[rows:]
    own_ref[1, :, kc] = dv[rows:]
    send_ref[0, :, kc] = dk[:rows].astype(send_ref.dtype)
    send_ref[1, :, kc] = dv[:rows].astype(send_ref.dtype)
    gains_ref[...] += jnp.concatenate([qterm, kterm], axis=0)


GROUPS_PER_STEP = 2


def window_attention(lo_rel, query_gain, key_gain, query_local, key_local, value_local, key_halo, value_halo, upstream,
                     ratio, head_dim):
    rows, query_width = query_local.shape
    key_width = key_local.shape[1]
    per_step = GROUPS_PER_STEP
    groups = key_width // (head_dim * per_step)
    kw = head_dim * per_step
    qw = ratio * kw
    keys = 2 * rows
    flops = 12 * rows * keys * head_dim * ratio * groups * per_step
    return pl.pallas_call(
        functools.partial(window_kernel, ratio, head_dim, per_step),
        grid=(groups,),
        in_specs=[
            pl.BlockSpec((rows, 1), lambda g: (0, 0)),
            pl.BlockSpec((1, head_dim), lambda g: (0, 0)),
            pl.BlockSpec((1, head_dim), lambda g: (0, 0)),
            pl.BlockSpec((rows, qw), lambda g: (0, g)),
            pl.BlockSpec((rows, kw), lambda g: (0, g)),
            pl.BlockSpec((rows, kw), lambda g: (0, g)),
            pl.BlockSpec((rows, kw), lambda g: (0, g)),
            pl.BlockSpec((rows, kw), lambda g: (0, g)),
            pl.BlockSpec((rows, qw), lambda g: (0, g)),
        ],
        out_specs=[
            pl.BlockSpec((rows, qw), lambda g: (0, g)),
            pl.BlockSpec((2, rows, kw), lambda g: (0, 0, g)),
            pl.BlockSpec((2, rows, kw), lambda g: (0, 0, g)),
            pl.BlockSpec((2, head_dim), lambda g: (0, 0)),
        ],
        out_shape=[
            jax.ShapeDtypeStruct((rows, query_width), jnp.bfloat16),
            jax.ShapeDtypeStruct((2, rows, key_width), jnp.float32),
            jax.ShapeDtypeStruct((2, rows, key_width), jnp.bfloat16),
            jax.ShapeDtypeStruct((2, head_dim), jnp.float32),
        ],
        cost_estimate=pl.CostEstimate(
            flops=flops,
            transcendentals=rows * keys * ratio * groups * per_step,
            bytes_accessed=2 * (4 * rows * query_width + 6 * rows * key_width) + 8 * rows * key_width,
        ),
    )(lo_rel, query_gain, key_gain, query_local, key_local, value_local, key_halo, value_halo, upstream)


def on_device(query_proj, key_proj, value_proj, out_grad, lowest_key_index, query_gain, key_gain):
    rows = query_proj.shape[2]
    query_width = query_proj.shape[3]
    key_width = key_proj.shape[3]
    head_dim = query_gain.shape[1]
    groups = key_width // head_dim
    heads = query_width // head_dim
    ratio = heads // groups
    query_local = query_proj.reshape(rows, query_width)
    key_local = key_proj.reshape(rows, key_width)
    value_local = value_proj.reshape(rows, key_width)
    pipe_devices = lax.axis_size("pipe")
    upstream = lax.ppermute(
        out_grad.reshape(rows, query_width), "pipe", [(i, (i - 1) % pipe_devices) for i in range(pipe_devices)]
    )
    key_halo = shifted(key_local, "seq", 1)
    value_halo = shifted(value_local, "seq", 1)
    block = lax.axis_index("seq")
    first = block * rows
    lo_rel = (lax.dynamic_slice(lowest_key_index.reshape(-1), (first,), (rows,)) - (first - rows)).reshape(rows, 1)
    key_scale = key_gain.reshape(head_dim)
    key_unit, key_inverse, _ = normalize(key_local.astype(jnp.float32).reshape(rows, groups, head_dim), key_scale)
    key_unit, key_inverse, query_local = lax.optimization_barrier((key_unit, key_inverse, query_local))
    query_grad, own, send, gain_terms = window_attention(
        lo_rel, query_gain, key_gain, query_local, key_local, value_local, key_halo, value_halo, upstream, ratio, head_dim
    )
    back = shifted(send, "seq", -1)
    received = gathered_over(gain_terms, ("dp", "seq"))
    key_normed_grad = (own[0] + back[0].astype(jnp.float32)).reshape(rows, groups, head_dim)
    value_rows = own[1] + back[1].astype(jnp.float32)
    key_grad = norm_back(key_normed_grad, key_unit, key_inverse, key_scale).astype(jnp.bfloat16)
    value_grad = value_rows.astype(jnp.bfloat16)
    key_grad, value_grad, received = lax.optimization_barrier((key_grad, value_grad, received))
    both = jnp.sum(received, axis=0)
    return (
        query_grad.reshape(1, 1, rows, query_width),
        key_grad.reshape(1, 1, rows, key_width),
        value_grad.reshape(1, 1, rows, key_width),
        both[0].reshape(1, head_dim),
        both[1].reshape(1, head_dim),
    )


def solution(mesh):
    return jax.shard_map(
        on_device,
        mesh=mesh,
        in_specs=(
            P("pipe", "dp", "seq", None),
            P("pipe", "dp", "seq", None),
            P("pipe", "dp", "seq", None),
            P("pipe", "dp", "seq", None),
            P("pipe", "dp", None),
            P("pipe", None),
            P("pipe", None),
        ),
        out_specs=(
            P("pipe", "dp", "seq", None),
            P("pipe", "dp", "seq", None),
            P("pipe", "dp", "seq", None),
            P("pipe", None),
            P("pipe", None),
        ),
        check_vma=False,
    )
```

```python
import functools

import jax
import jax.numpy as jnp
from jax import lax
from jax.experimental import pallas as pl
from jax.sharding import PartitionSpec as P

epsilon = 1e-06
score_scale = 168.0 ** (-0.5)


def gathered_over(x, axes):
    devices = 1
    for axis in axes:
        devices *= lax.axis_size(axis)
    copies = jnp.broadcast_to(x[None], (devices,) + x.shape)
    return lax.all_to_all(copies, axes, 0, 0, tiled=True)


def shifted(x, axis, by):
    devices = lax.axis_size(axis)
    pairs = [(i, i + by) for i in range(devices) if 0 <= i + by < devices]
    return lax.ppermute(x, axis, pairs)


def normalize(values, gain):
    inverse = lax.rsqrt(jnp.mean(values * values, axis=-1, keepdims=True) + epsilon)
    unit = values * inverse
    return (unit, inverse, (unit * gain).astype(jnp.bfloat16))


def norm_back(grad_normed, unit, inverse, gain):
    grad_unit = grad_normed * gain
    centered = grad_unit - unit * jnp.mean(grad_unit * unit, axis=-1, keepdims=True)
    return inverse * centered


def window_kernel(ratio, head_dim, per_step, lo_ref, qgain_ref, kgain_ref, q_ref, k_ref, v_ref, kh_ref, vh_ref,
                  up_ref, qgrad_ref, own_ref, send_ref, gains_ref):
    @pl.when(pl.program_id(0) == 0)
    def _():
        gains_ref[...] = jnp.zeros_like(gains_ref)

    for g in range(per_step):
        one_group(ratio, head_dim, g, lo_ref, qgain_ref, kgain_ref, q_ref, k_ref, v_ref, kh_ref, vh_ref, up_ref,
                  qgrad_ref, own_ref, send_ref, gains_ref)


def one_group(ratio, head_dim, g, lo_ref, qgain_ref, kgain_ref, q_ref, k_ref, v_ref, kh_ref, vh_ref, up_ref,
              qgrad_ref, own_ref, send_ref, gains_ref):
    rows = q_ref.shape[0]
    qgain = qgain_ref[...]
    kgain = kgain_ref[...]
    kc = slice(g * head_dim, (g + 1) * head_dim)
    key_raw = jnp.concatenate([kh_ref[:, kc], k_ref[:, kc]], axis=0).astype(jnp.float32)
    values = jnp.concatenate([vh_ref[:, kc], v_ref[:, kc]], axis=0)
    keys = key_raw.shape[0]
    key_unit, _, key_normed = normalize(key_raw, kgain)
    heads = [slice((g * ratio + h) * head_dim, (g * ratio + h + 1) * head_dim) for h in range(ratio)]
    query_unit, query_inverse, q = normalize(
        jnp.concatenate([q_ref[:, c] for c in heads], axis=0).astype(jnp.float32), qgain
    )
    up = jnp.concatenate([up_ref[:, c] for c in heads], axis=0)
    stacked = ratio * rows
    col = lax.broadcasted_iota(jnp.int32, (stacked, keys), 1)
    row = lax.broadcasted_iota(jnp.int32, (stacked, keys), 0) % rows
    lo = jnp.concatenate([lo_ref[...]] * ratio, axis=0)
    visible = (col >= lo) & (col <= row + (keys - rows))
    scores = lax.dot_general(q, key_normed, (((1,), (1,)), ((), ())), preferred_element_type=jnp.float32) * score_scale
    exp_scores = jnp.where(visible, jnp.exp(scores), 0.0)
    weights = exp_scores / jnp.sum(exp_scores, axis=-1, keepdims=True)
    weights_low = weights.astype(jnp.bfloat16)
    attended = jnp.dot(weights_low, values, preferred_element_type=jnp.float32)
    delta = jnp.sum(up.astype(jnp.float32) * attended, axis=-1, keepdims=True)
    prob_grad = lax.dot_general(up, values, (((1,), (1,)), ((), ())), preferred_element_type=jnp.float32)
    score_grad = weights * (prob_grad - delta) * score_scale
    dq = jnp.dot(score_grad.astype(jnp.bfloat16), key_normed, preferred_element_type=jnp.float32)
    query_grad = norm_back(dq, query_unit, query_inverse, qgain).astype(qgrad_ref.dtype)
    for h, c in enumerate(heads):
        qgrad_ref[:, c] = query_grad[h * rows:(h + 1) * rows]
    qterm = jnp.sum(dq * query_unit, axis=0, keepdims=True)
    dk = jnp.dot(score_grad.T.astype(jnp.bfloat16), q, preferred_element_type=jnp.float32)
    dv = jnp.dot(weights.T.astype(jnp.bfloat16), up, preferred_element_type=jnp.float32)
    kterm = jnp.sum(dk * key_unit, axis=0, keepdims=True)
    own_ref[0, :, kc] = dk[rows:]
    own_ref[1, :, kc] = dv[rows:]
    send_ref[0, :, kc] = dk[:rows].astype(send_ref.dtype)
    send_ref[1, :, kc] = dv[:rows].astype(send_ref.dtype)
    gains_ref[...] += jnp.concatenate([qterm, kterm], axis=0)


GROUPS_PER_STEP = 4


def window_attention(lo_rel, query_gain, key_gain, query_local, key_local, value_local, key_halo, value_halo, upstream,
                     ratio, head_dim):
    rows, query_width = query_local.shape
    key_width = key_local.shape[1]
    per_step = GROUPS_PER_STEP
    groups = key_width // (head_dim * per_step)
    kw = head_dim * per_step
    qw = ratio * kw
    keys = 2 * rows
    flops = 12 * rows * keys * head_dim * ratio * groups * per_step
    return pl.pallas_call(
        functools.partial(window_kernel, ratio, head_dim, per_step),
        grid=(groups,),
        in_specs=[
            pl.BlockSpec((rows, 1), lambda g: (0, 0)),
            pl.BlockSpec((1, head_dim), lambda g: (0, 0)),
            pl.BlockSpec((1, head_dim), lambda g: (0, 0)),
            pl.BlockSpec((rows, qw), lambda g: (0, g)),
            pl.BlockSpec((rows, kw), lambda g: (0, g)),
            pl.BlockSpec((rows, kw), lambda g: (0, g)),
            pl.BlockSpec((rows, kw), lambda g: (0, g)),
            pl.BlockSpec((rows, kw), lambda g: (0, g)),
            pl.BlockSpec((rows, qw), lambda g: (0, g)),
        ],
        out_specs=[
            pl.BlockSpec((rows, qw), lambda g: (0, g)),
            pl.BlockSpec((2, rows, kw), lambda g: (0, 0, g)),
            pl.BlockSpec((2, rows, kw), lambda g: (0, 0, g)),
            pl.BlockSpec((2, head_dim), lambda g: (0, 0)),
        ],
        out_shape=[
            jax.ShapeDtypeStruct((rows, query_width), jnp.bfloat16),
            jax.ShapeDtypeStruct((2, rows, key_width), jnp.float32),
            jax.ShapeDtypeStruct((2, rows, key_width), jnp.bfloat16),
            jax.ShapeDtypeStruct((2, head_dim), jnp.float32),
        ],
        cost_estimate=pl.CostEstimate(
            flops=flops,
            transcendentals=rows * keys * ratio * groups * per_step,
            bytes_accessed=2 * (4 * rows * query_width + 6 * rows * key_width) + 8 * rows * key_width,
        ),
    )(lo_rel, query_gain, key_gain, query_local, key_local, value_local, key_halo, value_halo, upstream)


def on_device(query_proj, key_proj, value_proj, out_grad, lowest_key_index, query_gain, key_gain):
    rows = query_proj.shape[2]
    query_width = query_proj.shape[3]
    key_width = key_proj.shape[3]
    head_dim = query_gain.shape[1]
    groups = key_width // head_dim
    heads = query_width // head_dim
    ratio = heads // groups
    query_local = query_proj.reshape(rows, query_width)
    key_local = key_proj.reshape(rows, key_width)
    value_local = value_proj.reshape(rows, key_width)
    pipe_devices = lax.axis_size("pipe")
    upstream = lax.ppermute(
        out_grad.reshape(rows, query_width), "pipe", [(i, (i - 1) % pipe_devices) for i in range(pipe_devices)]
    )
    key_halo = shifted(key_local, "seq", 1)
    value_halo = shifted(value_local, "seq", 1)
    block = lax.axis_index("seq")
    first = block * rows
    lo_rel = (lax.dynamic_slice(lowest_key_index.reshape(-1), (first,), (rows,)) - (first - rows)).reshape(rows, 1)
    key_scale = key_gain.reshape(head_dim)
    key_unit, key_inverse, _ = normalize(key_local.astype(jnp.float32).reshape(rows, groups, head_dim), key_scale)
    key_unit, key_inverse, query_local = lax.optimization_barrier((key_unit, key_inverse, query_local))
    query_grad, own, send, gain_terms = window_attention(
        lo_rel, query_gain, key_gain, query_local, key_local, value_local, key_halo, value_halo, upstream, ratio, head_dim
    )
    back = shifted(send, "seq", -1)
    received = gathered_over(gain_terms, ("dp", "seq"))
    key_normed_grad = (own[0] + back[0].astype(jnp.float32)).reshape(rows, groups, head_dim)
    value_rows = own[1] + back[1].astype(jnp.float32)
    key_grad = norm_back(key_normed_grad, key_unit, key_inverse, key_scale).astype(jnp.bfloat16)
    value_grad = value_rows.astype(jnp.bfloat16)
    key_grad, value_grad, received = lax.optimization_barrier((key_grad, value_grad, received))
    both = jnp.sum(received, axis=0)
    return (
        query_grad.reshape(1, 1, rows, query_width),
        key_grad.reshape(1, 1, rows, key_width),
        value_grad.reshape(1, 1, rows, key_width),
        both[0].reshape(1, head_dim),
        both[1].reshape(1, head_dim),
    )


def solution(mesh):
    return jax.shard_map(
        on_device,
        mesh=mesh,
        in_specs=(
            P("pipe", "dp", "seq", None),
            P("pipe", "dp", "seq", None),
            P("pipe", "dp", "seq", None),
            P("pipe", "dp", "seq", None),
            P("pipe", "dp", None),
            P("pipe", None),
            P("pipe", None),
        ),
        out_specs=(
            P("pipe", "dp", "seq", None),
            P("pipe", "dp", "seq", None),
            P("pipe", "dp", "seq", None),
            P("pipe", None),
            P("pipe", None),
        ),
        check_vma=False,
    )
```

```python
import functools

import jax
import jax.numpy as jnp
from jax import lax
from jax.experimental import pallas as pl
from jax.experimental.pallas import tpu as pltpu
from jax.sharding import PartitionSpec as P

epsilon = 1e-06
score_scale = 168.0 ** (-0.5)


def gathered_over(copies, axes):
    return lax.all_to_all(copies, axes, 0, 0, tiled=True)


def shifted(x, axis, by):
    devices = lax.axis_size(axis)
    pairs = [(i, i + by) for i in range(devices) if 0 <= i + by < devices]
    return lax.ppermute(x, axis, pairs)


def normalize(values, gain):
    inverse = lax.rsqrt(jnp.mean(values * values, axis=-1, keepdims=True) + epsilon)
    unit = values * inverse
    return (unit, inverse, (unit * gain).astype(jnp.bfloat16))


def norm_back(grad_normed, unit, inverse, gain):
    grad_unit = grad_normed * gain
    centered = grad_unit - unit * jnp.mean(grad_unit * unit, axis=-1, keepdims=True)
    return inverse * centered


def window_kernel(ratio, head_dim, per_step, lo_ref, qgain_ref, kgain_ref, q_ref, k_ref, v_ref, kh_ref, vh_ref,
                  up_ref, qgrad_ref, own_ref, send_ref, copies_ref, gains_ref):
    @pl.when(pl.program_id(0) == 0)
    def _():
        gains_ref[...] = jnp.zeros_like(gains_ref)

    for g in range(per_step):
        one_group(ratio, head_dim, g, lo_ref, qgain_ref, kgain_ref, q_ref, k_ref, v_ref, kh_ref, vh_ref, up_ref,
                  qgrad_ref, own_ref, send_ref, gains_ref)

    @pl.when(pl.program_id(0) == pl.num_programs(0) - 1)
    def _():
        copies_ref[...] = jnp.broadcast_to(gains_ref[...][None], copies_ref.shape)


def one_group(ratio, head_dim, g, lo_ref, qgain_ref, kgain_ref, q_ref, k_ref, v_ref, kh_ref, vh_ref, up_ref,
              qgrad_ref, own_ref, send_ref, gains_ref):
    rows = q_ref.shape[0]
    qgain = qgain_ref[...]
    kgain = kgain_ref[...]
    kc = slice(g * head_dim, (g + 1) * head_dim)
    key_raw = jnp.concatenate([kh_ref[:, kc], k_ref[:, kc]], axis=0).astype(jnp.float32)
    values = jnp.concatenate([vh_ref[:, kc], v_ref[:, kc]], axis=0)
    keys = key_raw.shape[0]
    key_unit, _, key_normed = normalize(key_raw, kgain)
    heads = [slice((g * ratio + h) * head_dim, (g * ratio + h + 1) * head_dim) for h in range(ratio)]
    query_unit, query_inverse, q = normalize(
        jnp.concatenate([q_ref[:, c] for c in heads], axis=0).astype(jnp.float32), qgain
    )
    up = jnp.concatenate([up_ref[:, c] for c in heads], axis=0)
    stacked = ratio * rows
    col = lax.broadcasted_iota(jnp.int32, (stacked, keys), 1)
    row = lax.broadcasted_iota(jnp.int32, (stacked, keys), 0) % rows
    lo = jnp.concatenate([lo_ref[...]] * ratio, axis=0)
    visible = (col >= lo) & (col <= row + (keys - rows))
    scores = lax.dot_general(q, key_normed, (((1,), (1,)), ((), ())), preferred_element_type=jnp.float32) * score_scale
    exp_scores = jnp.where(visible, jnp.exp(scores), 0.0)
    weights = exp_scores / jnp.sum(exp_scores, axis=-1, keepdims=True)
    weights_low = weights.astype(jnp.bfloat16)
    attended = jnp.dot(weights_low, values, preferred_element_type=jnp.float32)
    delta = jnp.sum(up.astype(jnp.float32) * attended, axis=-1, keepdims=True)
    prob_grad = lax.dot_general(up, values, (((1,), (1,)), ((), ())), preferred_element_type=jnp.float32)
    score_grad = weights * (prob_grad - delta) * score_scale
    dq = jnp.dot(score_grad.astype(jnp.bfloat16), key_normed, preferred_element_type=jnp.float32)
    query_grad = norm_back(dq, query_unit, query_inverse, qgain).astype(qgrad_ref.dtype)
    for h, c in enumerate(heads):
        qgrad_ref[:, c] = query_grad[h * rows:(h + 1) * rows]
    qterm = jnp.sum(dq * query_unit, axis=0, keepdims=True)
    dk = jnp.dot(score_grad.T.astype(jnp.bfloat16), q, preferred_element_type=jnp.float32)
    dv = jnp.dot(weights.T.astype(jnp.bfloat16), up, preferred_element_type=jnp.float32)
    kterm = jnp.sum(dk * key_unit, axis=0, keepdims=True)
    own_ref[0, :, kc] = dk[rows:]
    own_ref[1, :, kc] = dv[rows:]
    send_ref[0, :, kc] = dk[:rows].astype(send_ref.dtype)
    send_ref[1, :, kc] = dv[:rows].astype(send_ref.dtype)
    gains_ref[...] += jnp.concatenate([qterm, kterm], axis=0)


GROUPS_PER_STEP = 4


def window_attention(lo_rel, query_gain, key_gain, query_local, key_local, value_local, key_halo, value_halo, upstream,
                     ratio, head_dim, copies):
    rows, query_width = query_local.shape
    key_width = key_local.shape[1]
    per_step = GROUPS_PER_STEP
    groups = key_width // (head_dim * per_step)
    kw = head_dim * per_step
    qw = ratio * kw
    keys = 2 * rows
    flops = 12 * rows * keys * head_dim * ratio * groups * per_step
    return pl.pallas_call(
        functools.partial(window_kernel, ratio, head_dim, per_step),
        grid=(groups,),
        in_specs=[
            pl.BlockSpec((rows, 1), lambda g: (0, 0)),
            pl.BlockSpec((1, head_dim), lambda g: (0, 0)),
            pl.BlockSpec((1, head_dim), lambda g: (0, 0)),
            pl.BlockSpec((rows, qw), lambda g: (0, g)),
            pl.BlockSpec((rows, kw), lambda g: (0, g)),
            pl.BlockSpec((rows, kw), lambda g: (0, g)),
            pl.BlockSpec((rows, kw), lambda g: (0, g)),
            pl.BlockSpec((rows, kw), lambda g: (0, g)),
            pl.BlockSpec((rows, qw), lambda g: (0, g)),
        ],
        out_specs=[
            pl.BlockSpec((rows, qw), lambda g: (0, g)),
            pl.BlockSpec((2, rows, kw), lambda g: (0, 0, g)),
            pl.BlockSpec((2, rows, kw), lambda g: (0, 0, g)),
            pl.BlockSpec((copies, 2, head_dim), lambda g: (0, 0, 0)),
        ],
        out_shape=[
            jax.ShapeDtypeStruct((rows, query_width), jnp.bfloat16),
            jax.ShapeDtypeStruct((2, rows, key_width), jnp.float32),
            jax.ShapeDtypeStruct((2, rows, key_width), jnp.bfloat16),
            jax.ShapeDtypeStruct((copies, 2, head_dim), jnp.float32),
        ],
        scratch_shapes=[pltpu.VMEM((2, head_dim), jnp.float32)],
        cost_estimate=pl.CostEstimate(
            flops=flops,
            transcendentals=rows * keys * ratio * groups * per_step,
            bytes_accessed=2 * (4 * rows * query_width + 6 * rows * key_width) + 8 * rows * key_width,
        ),
    )(lo_rel, query_gain, key_gain, query_local, key_local, value_local, key_halo, value_halo, upstream)


def on_device(query_proj, key_proj, value_proj, out_grad, lowest_key_index, query_gain, key_gain):
    rows = query_proj.shape[2]
    query_width = query_proj.shape[3]
    key_width = key_proj.shape[3]
    head_dim = query_gain.shape[1]
    groups = key_width // head_dim
    heads = query_width // head_dim
    ratio = heads // groups
    query_local = query_proj.reshape(rows, query_width)
    key_local = key_proj.reshape(rows, key_width)
    value_local = value_proj.reshape(rows, key_width)
    pipe_devices = lax.axis_size("pipe")
    upstream = lax.ppermute(
        out_grad.reshape(rows, query_width), "pipe", [(i, (i - 1) % pipe_devices) for i in range(pipe_devices)]
    )
    key_halo = shifted(key_local, "seq", 1)
    value_halo = shifted(value_local, "seq", 1)
    block = lax.axis_index("seq")
    first = block * rows
    lo_rel = (lax.dynamic_slice(lowest_key_index.reshape(-1), (first,), (rows,)) - (first - rows)).reshape(rows, 1)
    key_scale = key_gain.reshape(head_dim)
    key_unit, key_inverse, _ = normalize(key_local.astype(jnp.float32).reshape(rows, groups, head_dim), key_scale)
    key_unit, key_inverse, query_local = lax.optimization_barrier((key_unit, key_inverse, query_local))
    query_grad, own, send, gain_terms = window_attention(
        lo_rel, query_gain, key_gain, query_local, key_local, value_local, key_halo, value_halo, upstream, ratio, head_dim,
        lax.axis_size("dp") * lax.axis_size("seq"),
    )
    back = shifted(send, "seq", -1)
    received = gathered_over(gain_terms, ("dp", "seq"))
    key_normed_grad = (own[0] + back[0].astype(jnp.float32)).reshape(rows, groups, head_dim)
    value_rows = own[1] + back[1].astype(jnp.float32)
    key_grad = norm_back(key_normed_grad, key_unit, key_inverse, key_scale).astype(jnp.bfloat16)
    value_grad = value_rows.astype(jnp.bfloat16)
    key_grad, value_grad, received = lax.optimization_barrier((key_grad, value_grad, received))
    both = jnp.sum(received, axis=0)
    return (
        query_grad.reshape(1, 1, rows, query_width),
        key_grad.reshape(1, 1, rows, key_width),
        value_grad.reshape(1, 1, rows, key_width),
        both[0].reshape(1, head_dim),
        both[1].reshape(1, head_dim),
    )


def solution(mesh):
    return jax.shard_map(
        on_device,
        mesh=mesh,
        in_specs=(
            P("pipe", "dp", "seq", None),
            P("pipe", "dp", "seq", None),
            P("pipe", "dp", "seq", None),
            P("pipe", "dp", "seq", None),
            P("pipe", "dp", None),
            P("pipe", None),
            P("pipe", None),
        ),
        out_specs=(
            P("pipe", "dp", "seq", None),
            P("pipe", "dp", "seq", None),
            P("pipe", "dp", "seq", None),
            P("pipe", None),
            P("pipe", None),
        ),
        check_vma=False,
    )
```
